32 devices in a mesh: dp: 8 (over y, x, core), tensor: 4 (over z).
Axes of the slice: x: 2, y: 2, z: 4, core: 2. Of those that a mesh axis runs over, the one named last changes fastest.
Arguments:
- hidden_in: bfloat16 [16, 1024, 2048], P('dp', 'tensor'), may hold values from -6 to 6
- keep_slot: int32 [16], P('dp'), may hold values 0 or 1
- out_grad: bfloat16 [16, 1024, 2048], P('dp', 'tensor'), may hold values from -8 to 8
- ln1_gain: bfloat16 [2048], replicated, may hold values from 0.5 to 1.5
- ln1_bias: bfloat16 [2048], replicated, may hold values from -1.25 to 1.25
- ln2_gain: bfloat16 [2048], replicated, may hold values from 0.5 to 1.5
- ln2_bias: bfloat16 [2048], replicated, may hold values from -1.25 to 1.25
- qkv_weight: bfloat16 [2048, 6144], P(None, 'tensor'), may hold values from -0.125 to 0.125
- qkv_bias: bfloat16 [8, 768], P('tensor'), may hold values from -0.625 to 0.625
- dense_weight: bfloat16 [2048, 2048], P('tensor'), may hold values from -0.75 to 0.75
- dense_bias: bfloat16 [2048], replicated, may hold values from -1.25 to 1.25
- fc1_weight: bfloat16 [2048, 8192], P(None, 'tensor'), may hold values from -0.125 to 0.125
- fc1_bias: bfloat16 [8192], P('tensor'), may hold values from -1.25 to 1.25
- fc2_weight: bfloat16 [8192, 2048], P('tensor'), may hold values from -0.0625 to 0.0625
- fc2_bias: bfloat16 [2048], replicated, may hold values from -1.25 to 1.25
Outputs:
- block_out: bfloat16 [16, 1024, 2048], P('dp', 'tensor')
- hidden_grad: float32 [16, 1024, 2048], P('dp', 'tensor')
- ln1_gain_grad: float32 [2048], P(('dp', 'tensor'))
- ln1_bias_grad: float32 [2048], P(('dp', 'tensor'))
- ln2_gain_grad: float32 [2048], P(('dp', 'tensor'))
- ln2_bias_grad: float32 [2048], P(('dp', 'tensor'))
- qkv_weight_grad: float32 [2048, 6144], P('dp', 'tensor')
- qkv_bias_grad: float32 [8, 768], P('tensor', 'dp')
- dense_weight_grad: float32 [2048, 2048], P('tensor', 'dp')
- dense_bias_grad: float32 [2048], P(('dp', 'tensor'))
- fc1_weight_grad: float32 [2048, 8192], P('dp', 'tensor')
- fc1_bias_grad: float32 [4, 2048], P('tensor', 'dp')
- fc2_weight_grad: float32 [8192, 2048], P('tensor', 'dp')
- fc2_bias_grad: float32 [2048], P(('dp', 'tensor'))
The draws below stay inside these ranges and needn't reach their ends.
All inputs are finite; a program needn't handle non-finite values. No bound on the sum of `keep_slot` on one device may be relied on, other than what follows from the above.
Results may differ from the reference program's by a relative error of at most 0.0092.
Values may be sent and summed in bfloat16 or wider, within the bound.
No kernel may reach another device: no remote copies, remote signals or barrier semaphores. Data moves between devices by JAX's collectives and lax.ppermute only.
A program may use at most 320 MiB of HBM per device.

```python
import math
import jax
import jax.numpy as jnp
from jax import lax

D = 2048
HEADS = 8
HD = 256
ROT = 64
FF = 8192
SEQ = 1024
ROWS = 16
N_TENSOR = 4


def touch_ends(entries, own_key, smallest, largest):
    place = [jax.random.randint(jax.random.fold_in(own_key, axis), (), 0, length) for axis, length in enumerate(entries.shape)]
    longest = entries.shape.index(max(entries.shape))
    neighbour = place[:longest] + [(place[longest] + 1) % entries.shape[longest]] + place[longest + 1:]
    return entries.at[tuple(place)].set(smallest).at[tuple(neighbour)].set(largest)


def strengthened(array, own_key, source, target, shards_of, factor):
    owner, partner = [(jnp.arange(array.shape[position]) // (array.shape[position] // shards_of)).reshape([-1 if axis == position else 1 for axis in range(array.ndim)]) for position in (source, target)]
    chosen = jax.random.permutation(own_key, shards_of)[partner]
    strong = (owner == chosen) | (owner == (partner + shards_of // 2) % shards_of)
    return jnp.where(strong, factor * array, array)


def block_levels(key, extent, cuts, low, high):
    gain = 1.0
    for position, shards_of in cuts:
        heights = jax.random.uniform(jax.random.fold_in(jax.random.fold_in(key, 6), position), (shards_of,), jnp.float32, low / len(cuts), high / len(cuts))
        gain = gain * jnp.repeat(jnp.exp(heights), extent[position] // shards_of).reshape((-1,) + (1,) * (len(extent) - 1 - position))
    return gain


def bell_draw(stream_key, shape, width, bound, shards=(), kind=jnp.bfloat16):
    entries = jax.random.normal(stream_key, shape, jnp.float32) * width
    if len(shards) > 0:
        entries = block_levels(stream_key, shape, shards, -0.22, 0.18) * entries
    return jnp.clip(entries, min=-bound, max=bound).astype(kind)


def bell_draw_with(key, shape, spread, limit, cuts, heavy, kind=jnp.bfloat16):
    values = spread * jax.random.normal(key, shape, jnp.float32)
    if cuts:
        values = values * block_levels(key, shape, cuts, -0.22, 0.18)
    return jnp.clip(strengthened(values, jax.random.fold_in(key, 3), *heavy), -limit, limit).astype(kind)


def setup_inputs(seed: int = 0) -> dict:
    arg_keys = jax.random.split(jax.random.key(seed), 16)
    return {
        "hidden_in": bell_draw(arg_keys[0], (ROWS, SEQ, D), 1.0, 6.0, ((0, 8), (1, 4))),
        "keep_slot": touch_ends((jax.random.randint(arg_keys[1], (ROWS,), 0, 4) < 3).astype(jnp.int32), jax.random.fold_in(arg_keys[1], 1), 0, 1),
        "out_grad": bell_draw_with(arg_keys[2], (ROWS, SEQ, D), 1.0, 8.0, ((0, 8), (1, 4)), (0, 2, 8, 2.0)),
        "ln1_gain": jnp.clip(1.0 + 0.1 * jax.random.normal(arg_keys[3], (D,), jnp.float32), 0.5, 1.5).astype(jnp.bfloat16),
        "ln1_bias": bell_draw(arg_keys[4], (D,), 0.2, 1.25),
        "ln2_gain": jnp.clip(1.0 + 0.1 * jax.random.normal(arg_keys[5], (D,), jnp.float32), 0.5, 1.5).astype(jnp.bfloat16),
        "ln2_bias": bell_draw(arg_keys[6], (D,), 0.2, 1.25),
        "qkv_weight": bell_draw(arg_keys[7], (D, HEADS * 3 * HD), D ** -0.5, 0.125, ((1, 4),)),
        "qkv_bias": bell_draw(arg_keys[8], (HEADS, 3 * HD), 0.1, 0.625, ((0, 4),)),
        "dense_weight": bell_draw(arg_keys[9], (HEADS * HD, D), (max(HEADS * HD // 32, 1)) ** -0.5, 0.75, ((0, 4),)),
        "dense_bias": bell_draw(arg_keys[10], (D,), 0.2, 1.25),
        "fc1_weight": bell_draw(arg_keys[11], (D, FF), D ** -0.5, 0.125, ((1, 4),)),
        "fc1_bias": bell_draw(arg_keys[12], (FF,), 0.2, 1.25, ((0, 4),)),
        "fc2_weight": bell_draw(arg_keys[13], (FF, D), FF ** -0.5, 0.0625, ((0, 4),)),
        "fc2_bias": bell_draw(arg_keys[14], (D,), 0.2, 1.25),
    }


layer_eps = 1e-05
rope_base = 10000.0
mask_fill = -1e+30

@jax.custom_vjp
def low(v):
    return lax.optimization_barrier(v.astype(jnp.bfloat16)).astype(jnp.float32)

@jax.custom_vjp
def low_back(v):
    return v

def low_keep(v):
    return (low(v), None)

def low_pass(kept, grad):
    return (grad,)

def back_keep(v):
    return (v, None)

def back_low(kept, grad):
    return (low(grad),)
low.defvjp(low_keep, low_pass)
low_back.defvjp(back_keep, back_low)

def matmul(left, right):
    return jnp.dot(left, right, precision=lax.Precision.HIGHEST, preferred_element_type=jnp.float32)

def rope_tables(length, rot_dims):
    half = rot_dims // 2
    freqs = jnp.exp(-jnp.log(rope_base) * (2.0 * jnp.arange(half, dtype=jnp.float32) / rot_dims))
    angles = jnp.arange(length, dtype=jnp.float32)[:, None] * freqs[None, :]
    return (jnp.cos(angles), jnp.sin(angles))

def rotate(field, cosine, sine, rot_dims, sign):
    half = rot_dims // 2
    first = field[..., :half]
    second = field[..., half:rot_dims]
    rest = field[..., rot_dims:]
    cos_b = cosine[:, None, :]
    sin_b = sign * sine[:, None, :]
    return jnp.concatenate([first * cos_b - second * sin_b, second * cos_b + first * sin_b, rest], axis=-1)

def gelu_exact(field):
    return jax.nn.gelu(field, approximate=False)

def forward_row(rows, keep, params):
    gain_one, shift_one, gain_two, shift_two, w_qkv, b_qkv, w_dense, b_dense, w_up, b_up, w_down, b_down = params
    centred = rows - lax.optimization_barrier(jnp.mean(rows, axis=-1, keepdims=True))
    normed = centred * lax.rsqrt(lax.optimization_barrier(jnp.mean(centred * centred, axis=-1, keepdims=True)) + layer_eps)
    normed_one = low(normed * gain_one + shift_one)
    normed_two = low(normed * gain_two + shift_two)
    joined = low_back(matmul(normed_one, w_qkv) + b_qkv.reshape(-1)).reshape(SEQ, HEADS, 3, HD)
    cosine, sine = rope_tables(SEQ, ROT)
    query_rot = low(rotate(joined[:, :, 0], cosine, sine, ROT, 1.0))
    key_rot = low(rotate(joined[:, :, 1], cosine, sine, ROT, 1.0))
    value_rows = low(joined[:, :, 2])
    scale = 1.0 / math.sqrt(HD)
    scores = low_back(jnp.einsum('qhd,khd->hqk', query_rot, key_rot, precision=lax.Precision.HIGHEST) * scale)
    positions = jnp.arange(SEQ)
    allowed = positions[None, :] <= positions[:, None]
    scores = jnp.where(allowed[None], scores, mask_fill)
    probs = jax.nn.softmax(scores, axis=-1)
    mixed = jnp.einsum('hqk,khd->qhd', low(probs), value_rows, precision=lax.Precision.HIGHEST)
    mixed = low(low_back(mixed)).reshape(SEQ, HEADS * HD)
    attn_out = matmul(mixed, w_dense)
    pre_act = low_back(matmul(normed_two, w_up) + b_up)
    act_low = low(gelu_exact(pre_act))
    branch = low_back(attn_out + matmul(act_low, w_down) + b_dense + b_down)
    return rows + keep * branch

def reference(hidden_in, keep_slot, out_grad, ln1_gain, ln1_bias, ln2_gain, ln2_bias, qkv_weight, qkv_bias, dense_weight, dense_bias, fc1_weight, fc1_bias, fc2_weight, fc2_bias):
    params = tuple((item.astype(jnp.float32) for item in (ln1_gain, ln1_bias, ln2_gain, ln2_bias, qkv_weight, qkv_bias, dense_weight, dense_bias, fc1_weight, fc1_bias, fc2_weight, fc2_bias)))
    keep_all = keep_slot.astype(jnp.float32)

    def step(totals, inputs):
        rows, keep, cotangent = inputs
        result, pull = jax.vjp(lambda row_vals, prm: forward_row(row_vals, keep, prm), rows.astype(jnp.float32), params)
        row_grad, param_grads = pull(cotangent.astype(jnp.float32))
        totals = tuple((a + b for a, b in zip(totals, param_grads)))
        return (totals, (result.astype(jnp.bfloat16), row_grad))
    zeros = tuple((jnp.zeros(item.shape, jnp.float32) for item in params))
    totals, outputs = lax.scan(step, zeros, (hidden_in, keep_all, out_grad))
    block_out, hidden_grad = outputs
    return (block_out, hidden_grad, totals[0], totals[1], totals[2], totals[3], totals[4], totals[5], totals[6], totals[7], totals[8], totals[9].reshape(N_TENSOR, FF // N_TENSOR), totals[10], totals[11])
```

```python
import math

import jax
import jax.numpy as jnp
from jax import lax
from jax.sharding import PartitionSpec as P

ROT = 64


layer_eps = 1e-05
rope_base = 10000.0
mask_fill = -1e30


def rope_tables(length, rot_dims):
    half = rot_dims // 2
    freqs = jnp.exp(-jnp.log(rope_base) * (2.0 * jnp.arange(half, dtype=jnp.float32) / rot_dims))
    angles = jnp.arange(length, dtype=jnp.float32)[:, None] * freqs[None, :]
    return (jnp.cos(angles), jnp.sin(angles))


def rotate(field, cosine, sine, rot_dims, sign):
    half = rot_dims // 2
    first = field[..., :half]
    second = field[..., half:rot_dims]
    rest = field[..., rot_dims:]
    cos_b = cosine[None, :, None, :]
    sin_b = sign * sine[None, :, None, :]
    return jnp.concatenate(
        [first * cos_b - second * sin_b, second * cos_b + first * sin_b, rest], axis=-1
    )


def gelu_exact(field):
    return jax.nn.gelu(field, approximate=False)


def mm(left, right, dims):
    return lax.dot_general(left, right, (dims, ((), ())), preferred_element_type=jnp.float32)


def local(
    hidden_in,
    keep_slot,
    out_grad,
    ln1_gain,
    ln1_bias,
    ln2_gain,
    ln2_bias,
    qkv_weight,
    qkv_bias,
    dense_weight,
    dense_bias,
    fc1_weight,
    fc1_bias,
    fc2_weight,
    fc2_bias,
):
    slots, own_len, width = hidden_in.shape
    seq_len = own_len * lax.axis_size("tensor")
    head_local, three_hd = qkv_bias.shape
    head_dim = three_hd // 3
    ff_local = fc1_weight.shape[1]
    scale = 1.0 / math.sqrt(head_dim)
    keep = keep_slot.astype(jnp.float32)[:, None, None]

    inputs_all = lax.all_gather(hidden_in, "tensor", axis=1, tiled=True)
    grads_all = lax.all_gather(out_grad, "tensor", axis=1, tiled=True)
    cosine, sine = rope_tables(seq_len, ROT)

    rows = inputs_all.astype(jnp.float32)
    centred = rows - jnp.mean(rows, axis=-1, keepdims=True)
    inv_std = lax.rsqrt(jnp.mean(centred * centred, axis=-1, keepdims=True) + layer_eps)
    normed = centred * inv_std
    g1 = ln1_gain.astype(jnp.float32)
    g2 = ln2_gain.astype(jnp.float32)
    normed_one = (normed * g1 + ln1_bias.astype(jnp.float32)).astype(jnp.bfloat16)
    normed_two = (normed * g2 + ln2_bias.astype(jnp.float32)).astype(jnp.bfloat16)

    joined = mm(normed_one, qkv_weight, ((2,), (0,))) + qkv_bias.reshape(-1).astype(jnp.float32)
    joined = joined.reshape(slots, seq_len, head_local, 3, head_dim)
    query_rot = rotate(joined[:, :, :, 0], cosine, sine, ROT, 1.0).astype(jnp.bfloat16)
    key_rot = rotate(joined[:, :, :, 1], cosine, sine, ROT, 1.0).astype(jnp.bfloat16)
    value_rows = joined[:, :, :, 2].astype(jnp.bfloat16)

    pos = jnp.arange(seq_len)
    allowed = (pos[None, :] <= pos[:, None])[None, None]
    scores = jnp.einsum(
        "sqhd,skhd->shqk", query_rot, key_rot, preferred_element_type=jnp.float32
    ) * scale
    scores = jnp.where(allowed, scores, mask_fill)
    top = jnp.max(scores, axis=-1, keepdims=True)
    weights = jnp.exp(scores - top)
    total = jnp.sum(weights, axis=-1, keepdims=True)
    probs = weights / total
    probs_low = probs.astype(jnp.bfloat16)
    mixed = jnp.einsum(
        "shqk,skhd->sqhd", probs_low, value_rows, preferred_element_type=jnp.float32
    )
    attn_rows = mixed.astype(jnp.bfloat16).reshape(slots, seq_len, head_local * head_dim)

    pre_act = mm(normed_two, fc1_weight, ((2,), (0,))) + fc1_bias.astype(jnp.float32)
    act_val, act_back = jax.vjp(gelu_exact, pre_act)
    act_low = act_val.astype(jnp.bfloat16)
    partial_out = mm(attn_rows, dense_weight, ((2,), (0,))) + mm(act_low, fc2_weight, ((2,), (0,)))
    branch_own = lax.psum_scatter(partial_out, "tensor", scatter_dimension=1, tiled=True)
    branch_own = branch_own + dense_bias.astype(jnp.float32) + fc2_bias.astype(jnp.float32)
    own_in = hidden_in.astype(jnp.float32)
    block_out = (own_in + keep * branch_own).astype(jnp.bfloat16)

    keep_low = keep_slot.astype(jnp.bfloat16)[:, None, None]
    branch_grad = grads_all * keep_low
    own_cot = out_grad.astype(jnp.float32)
    out_bias_part = jnp.sum(own_cot * keep, axis=(0, 1))

    down_grad = mm(act_low, branch_grad, ((0, 1), (0, 1)))
    dense_grad = mm(attn_rows, branch_grad, ((0, 1), (0, 1)))
    act_grad = mm(branch_grad, fc2_weight, ((2,), (1,)))
    pre_grad = act_back(act_grad)[0].astype(jnp.bfloat16)
    up_bias_grad = jnp.sum(pre_grad.astype(jnp.float32), axis=(0, 1))
    up_grad = mm(normed_two, pre_grad, ((0, 1), (0, 1)))
    normed_two_grad = mm(pre_grad, fc1_weight, ((2,), (1,)))
    mixed_grad = mm(branch_grad, dense_weight, ((2,), (1,))).astype(jnp.bfloat16)
    mixed_grad = mixed_grad.reshape(slots, seq_len, head_local, head_dim)

    prob_grad = jnp.einsum(
        "sqhd,skhd->shqk", mixed_grad, value_rows, preferred_element_type=jnp.float32
    )
    inner = jnp.sum(probs * prob_grad, axis=-1, keepdims=True)
    score_grad = (probs * (prob_grad - inner)).astype(jnp.bfloat16)
    query_grad = jnp.einsum(
        "shqk,skhd->sqhd", score_grad, key_rot, preferred_element_type=jnp.float32
    ) * scale
    key_grad = jnp.einsum(
        "shqk,sqhd->skhd", score_grad, query_rot, preferred_element_type=jnp.float32
    ) * scale
    value_grad = jnp.einsum(
        "shqk,sqhd->skhd", probs_low, mixed_grad, preferred_element_type=jnp.float32
    )
    query_grad = rotate(query_grad, cosine, sine, ROT, -1.0)
    key_grad = rotate(key_grad, cosine, sine, ROT, -1.0)
    joined_grad = (
        jnp.stack([query_grad, key_grad, value_grad], axis=3)
        .reshape(slots, seq_len, head_local * three_hd)
        .astype(jnp.bfloat16)
    )
    qkv_bias_grad = jnp.sum(joined_grad.astype(jnp.float32), axis=(0, 1))
    qkv_grad = mm(normed_one, joined_grad, ((0, 1), (0, 1)))
    normed_one_grad = mm(joined_grad, qkv_weight, ((2,), (1,)))

    gain_one = jnp.sum(normed_one_grad * normed, axis=(0, 1))
    shift_one = jnp.sum(normed_one_grad, axis=(0, 1))
    gain_two = jnp.sum(normed_two_grad * normed, axis=(0, 1))
    shift_two = jnp.sum(normed_two_grad, axis=(0, 1))
    normed_grad = normed_one_grad * g1 + normed_two_grad * g2
    own_grad = lax.psum_scatter(
        normed_grad.astype(jnp.bfloat16), "tensor", scatter_dimension=1, tiled=True
    ).astype(jnp.float32)

    own_c = own_in - jnp.mean(own_in, axis=-1, keepdims=True)
    own_inv = lax.rsqrt(jnp.mean(own_c * own_c, axis=-1, keepdims=True) + layer_eps)
    own_normed = own_c * own_inv
    back_rows = own_inv * (
        own_grad
        - jnp.mean(own_grad, axis=-1, keepdims=True)
        - own_normed * jnp.mean(own_grad * own_normed, axis=-1, keepdims=True)
    )
    hidden_grad = own_cot + back_rows

    weight_parts = (
        lax.psum_scatter(qkv_grad, "dp", scatter_dimension=0, tiled=True),
        lax.psum_scatter(dense_grad, "dp", scatter_dimension=1, tiled=True),
        lax.psum_scatter(up_grad, "dp", scatter_dimension=0, tiled=True),
        lax.psum_scatter(down_grad, "dp", scatter_dimension=1, tiled=True),
        lax.psum_scatter(
            qkv_bias_grad.reshape(head_local, three_hd), "dp", scatter_dimension=1, tiled=True
        ),
        lax.psum_scatter(up_bias_grad.reshape(1, -1), "dp", scatter_dimension=1, tiled=True),
    )
    small_parts = lax.psum_scatter(
        jnp.stack([gain_one, shift_one, gain_two, shift_two, out_bias_part]),
        ("dp", "tensor"),
        scatter_dimension=1,
        tiled=True,
    )
    return (
        block_out,
        hidden_grad,
        small_parts[0],
        small_parts[1],
        small_parts[2],
        small_parts[3],
        weight_parts[0],
        weight_parts[4],
        weight_parts[1],
        small_parts[4],
        weight_parts[2],
        weight_parts[5],
        weight_parts[3],
        small_parts[4],
    )


def solution(mesh):
    in_specs = (
        P("dp", "tensor", None),
        P("dp"),
        P("dp", "tensor", None),
        P(),
        P(),
        P(),
        P(),
        P(None, "tensor"),
        P("tensor", None),
        P("tensor", None),
        P(),
        P(None, "tensor"),
        P("tensor"),
        P("tensor", None),
        P(),
    )
    out_specs = (
        P("dp", "tensor", None),
        P("dp", "tensor", None),
        P(("dp", "tensor")),
        P(("dp", "tensor")),
        P(("dp", "tensor")),
        P(("dp", "tensor")),
        P("dp", "tensor"),
        P("tensor", "dp"),
        P("tensor", "dp"),
        P(("dp", "tensor")),
        P("dp", "tensor"),
        P("tensor", "dp"),
        P("tensor", "dp"),
        P(("dp", "tensor")),
    )
    return jax.shard_map(local, mesh=mesh, in_specs=in_specs, out_specs=out_specs, check_vma=False)
```

```python
import math

import jax
import jax.numpy as jnp
from jax import lax
from jax.sharding import PartitionSpec as P

ROT = 64


layer_eps = 1e-05
rope_base = 10000.0
mask_fill = -1e30


def rope_tables(length, rot_dims):
    half = rot_dims // 2
    freqs = jnp.exp(-jnp.log(rope_base) * (2.0 * jnp.arange(half, dtype=jnp.float32) / rot_dims))
    angles = jnp.arange(length, dtype=jnp.float32)[:, None] * freqs[None, :]
    return (jnp.cos(angles), jnp.sin(angles))


def rotate(field, cosine, sine, rot_dims, sign):
    half = rot_dims // 2
    first = field[..., :half]
    second = field[..., half:rot_dims]
    rest = field[..., rot_dims:]
    cos_b = cosine[None, :, None, :]
    sin_b = sign * sine[None, :, None, :]
    return jnp.concatenate(
        [first * cos_b - second * sin_b, second * cos_b + first * sin_b, rest], axis=-1
    )


def gelu_exact(field):
    return jax.nn.gelu(field, approximate=False)


def mm(left, right, dims):
    return lax.dot_general(left, right, (dims, ((), ())), preferred_element_type=jnp.float32)


def line_all_gather(x, axis_name):
    n = lax.axis_size(axis_name)
    idx = lax.axis_index(axis_name)
    own = x.shape[1]
    right, left = x, x
    rights, lefts = [], []
    for s in range(1, n):
        right = lax.ppermute(right, axis_name, [(i, i + 1) for i in range(s - 1, n - 1)])
        left = lax.ppermute(left, axis_name, [(i, i - 1) for i in range(1, n - s + 1)])
        rights.append(right)
        lefts.append(left)
    rel = jnp.concatenate(rights[::-1] + [x] + lefts, axis=1)
    return lax.dynamic_slice_in_dim(rel, (n - 1 - idx) * own, n * own, axis=1)


def line_reduce_scatter(p, axis_name, send_dtype):
    n = lax.axis_size(axis_name)
    idx = lax.axis_index(axis_name)
    own = p.shape[1] // n

    def chunk(k):
        k = jnp.clip(k, 0, n - 1)
        return lax.dynamic_slice_in_dim(p, k * own, own, axis=1).astype(jnp.float32)

    recv_r = None
    recv_l = None
    for s in range(1, n):
        send_r = chunk(idx + n - s)
        send_l = chunk(idx - n + s)
        if recv_r is not None:
            send_r = send_r + recv_r.astype(jnp.float32)
            send_l = send_l + recv_l.astype(jnp.float32)
        recv_r = lax.ppermute(
            send_r.astype(send_dtype), axis_name, [(i, i + 1) for i in range(0, min(s, n - 1))]
        )
        recv_l = lax.ppermute(
            send_l.astype(send_dtype), axis_name, [(i, i - 1) for i in range(max(n - s, 1), n)]
        )
    out = chunk(idx)
    if recv_r is not None:
        out = out + recv_r.astype(jnp.float32) + recv_l.astype(jnp.float32)
    return out


def local(
    hidden_in,
    keep_slot,
    out_grad,
    ln1_gain,
    ln1_bias,
    ln2_gain,
    ln2_bias,
    qkv_weight,
    qkv_bias,
    dense_weight,
    dense_bias,
    fc1_weight,
    fc1_bias,
    fc2_weight,
    fc2_bias,
):
    slots, own_len, width = hidden_in.shape
    seq_len = own_len * lax.axis_size("tensor")
    head_local, three_hd = qkv_bias.shape
    head_dim = three_hd // 3
    ff_local = fc1_weight.shape[1]
    scale = 1.0 / math.sqrt(head_dim)
    keep = keep_slot.astype(jnp.float32)[:, None, None]

    inputs_all = line_all_gather(hidden_in, "tensor")
    inputs_all, out_grad_b = lax.optimization_barrier((inputs_all, out_grad))
    grads_all = line_all_gather(out_grad_b, "tensor")
    cosine, sine = rope_tables(seq_len, ROT)

    rows = inputs_all.astype(jnp.float32)
    centred = rows - jnp.mean(rows, axis=-1, keepdims=True)
    inv_std = lax.rsqrt(jnp.mean(centred * centred, axis=-1, keepdims=True) + layer_eps)
    normed = centred * inv_std
    g1 = ln1_gain.astype(jnp.float32)
    g2 = ln2_gain.astype(jnp.float32)
    normed_one = (normed * g1 + ln1_bias.astype(jnp.float32)).astype(jnp.bfloat16)
    normed_two = (normed * g2 + ln2_bias.astype(jnp.float32)).astype(jnp.bfloat16)

    joined = mm(normed_one, qkv_weight, ((2,), (0,))) + qkv_bias.reshape(-1).astype(jnp.float32)
    joined = joined.reshape(slots, seq_len, head_local, 3, head_dim)
    query_rot = rotate(joined[:, :, :, 0], cosine, sine, ROT, 1.0).astype(jnp.bfloat16)
    key_rot = rotate(joined[:, :, :, 1], cosine, sine, ROT, 1.0).astype(jnp.bfloat16)
    value_rows = joined[:, :, :, 2].astype(jnp.bfloat16)

    pos = jnp.arange(seq_len)
    allowed = (pos[None, :] <= pos[:, None])[None, None]
    scores = jnp.einsum(
        "sqhd,skhd->shqk", query_rot, key_rot, preferred_element_type=jnp.float32
    ) * scale
    scores = jnp.where(allowed, scores, mask_fill)
    top = jnp.max(scores, axis=-1, keepdims=True)
    weights = jnp.exp(scores - top)
    total = jnp.sum(weights, axis=-1, keepdims=True)
    probs = weights / total
    probs_low = probs.astype(jnp.bfloat16)
    mixed = jnp.einsum(
        "shqk,skhd->sqhd", probs_low, value_rows, preferred_element_type=jnp.float32
    )
    attn_rows = mixed.astype(jnp.bfloat16).reshape(slots, seq_len, head_local * head_dim)

    pre_act = mm(normed_two, fc1_weight, ((2,), (0,))) + fc1_bias.astype(jnp.float32)
    act_val, act_back = jax.vjp(gelu_exact, pre_act)
    act_low = act_val.astype(jnp.bfloat16)
    partial_out = mm(attn_rows, dense_weight, ((2,), (0,))) + mm(act_low, fc2_weight, ((2,), (0,)))
    branch_own = line_reduce_scatter(partial_out, "tensor", jnp.float32)
    branch_own = branch_own + dense_bias.astype(jnp.float32) + fc2_bias.astype(jnp.float32)
    own_in = hidden_in.astype(jnp.float32)
    block_out = (own_in + keep * branch_own).astype(jnp.bfloat16)

    keep_low = keep_slot.astype(jnp.bfloat16)[:, None, None]
    branch_grad = grads_all * keep_low
    own_cot = out_grad.astype(jnp.float32)
    out_bias_part = jnp.sum(own_cot * keep, axis=(0, 1))

    down_grad = mm(act_low, branch_grad, ((0, 1), (0, 1)))
    dense_grad = mm(attn_rows, branch_grad, ((0, 1), (0, 1)))
    down_grad, dense_grad, branch_grad = lax.optimization_barrier(
        (down_grad, dense_grad, branch_grad)
    )
    act_grad = mm(branch_grad, fc2_weight, ((2,), (1,)))
    pre_grad = act_back(act_grad)[0].astype(jnp.bfloat16)
    up_bias_grad = jnp.sum(pre_grad.astype(jnp.float32), axis=(0, 1))
    up_grad = mm(normed_two, pre_grad, ((0, 1), (0, 1)))
    up_grad, pre_grad = lax.optimization_barrier((up_grad, pre_grad))
    normed_two_grad = mm(pre_grad, fc1_weight, ((2,), (1,)))
    mixed_grad = mm(branch_grad, dense_weight, ((2,), (1,))).astype(jnp.bfloat16)
    mixed_grad = mixed_grad.reshape(slots, seq_len, head_local, head_dim)

    prob_grad = jnp.einsum(
        "sqhd,skhd->shqk", mixed_grad, value_rows, preferred_element_type=jnp.float32
    )
    inner = jnp.sum(probs * prob_grad, axis=-1, keepdims=True)
    score_grad = (probs * (prob_grad - inner)).astype(jnp.bfloat16)
    query_grad = jnp.einsum(
        "shqk,skhd->sqhd", score_grad, key_rot, preferred_element_type=jnp.float32
    ) * scale
    key_grad = jnp.einsum(
        "shqk,sqhd->skhd", score_grad, query_rot, preferred_element_type=jnp.float32
    ) * scale
    value_grad = jnp.einsum(
        "shqk,sqhd->skhd", probs_low, mixed_grad, preferred_element_type=jnp.float32
    )
    query_grad = rotate(query_grad, cosine, sine, ROT, -1.0)
    key_grad = rotate(key_grad, cosine, sine, ROT, -1.0)
    joined_grad = (
        jnp.stack([query_grad, key_grad, value_grad], axis=3)
        .reshape(slots, seq_len, head_local * three_hd)
        .astype(jnp.bfloat16)
    )
    qkv_bias_grad = jnp.sum(joined_grad.astype(jnp.float32), axis=(0, 1))
    qkv_grad = mm(normed_one, joined_grad, ((0, 1), (0, 1)))
    qkv_grad, joined_grad = lax.optimization_barrier((qkv_grad, joined_grad))
    normed_one_grad = mm(joined_grad, qkv_weight, ((2,), (1,)))

    gain_one = jnp.sum(normed_one_grad * normed, axis=(0, 1))
    shift_one = jnp.sum(normed_one_grad, axis=(0, 1))
    gain_two = jnp.sum(normed_two_grad * normed, axis=(0, 1))
    shift_two = jnp.sum(normed_two_grad, axis=(0, 1))
    normed_grad = normed_one_grad * g1 + normed_two_grad * g2
    own_grad = line_reduce_scatter(normed_grad, "tensor", jnp.bfloat16)

    own_c = own_in - jnp.mean(own_in, axis=-1, keepdims=True)
    own_inv = lax.rsqrt(jnp.mean(own_c * own_c, axis=-1, keepdims=True) + layer_eps)
    own_normed = own_c * own_inv
    back_rows = own_inv * (
        own_grad
        - jnp.mean(own_grad, axis=-1, keepdims=True)
        - own_normed * jnp.mean(own_grad * own_normed, axis=-1, keepdims=True)
    )
    hidden_grad = own_cot + back_rows

    weight_parts = (
        lax.psum_scatter(qkv_grad, "dp", scatter_dimension=0, tiled=True),
        lax.psum_scatter(dense_grad, "dp", scatter_dimension=1, tiled=True),
        lax.psum_scatter(up_grad, "dp", scatter_dimension=0, tiled=True),
        lax.psum_scatter(down_grad, "dp", scatter_dimension=1, tiled=True),
        lax.psum_scatter(
            qkv_bias_grad.reshape(head_local, three_hd), "dp", scatter_dimension=1, tiled=True
        ),
        lax.psum_scatter(up_bias_grad.reshape(1, -1), "dp", scatter_dimension=1, tiled=True),
    )
    small_parts = lax.psum_scatter(
        jnp.stack([gain_one, shift_one, gain_two, shift_two, out_bias_part]),
        ("dp", "tensor"),
        scatter_dimension=1,
        tiled=True,
    )
    return (
        block_out,
        hidden_grad,
        small_parts[0],
        small_parts[1],
        small_parts[2],
        small_parts[3],
        weight_parts[0],
        weight_parts[4],
        weight_parts[1],
        small_parts[4],
        weight_parts[2],
        weight_parts[5],
        weight_parts[3],
        small_parts[4],
    )


def solution(mesh):
    in_specs = (
        P("dp", "tensor", None),
        P("dp"),
        P("dp", "tensor", None),
        P(),
        P(),
        P(),
        P(),
        P(None, "tensor"),
        P("tensor", None),
        P("tensor", None),
        P(),
        P(None, "tensor"),
        P("tensor"),
        P("tensor", None),
        P(),
    )
    out_specs = (
        P("dp", "tensor", None),
        P("dp", "tensor", None),
        P(("dp", "tensor")),
        P(("dp", "tensor")),
        P(("dp", "tensor")),
        P(("dp", "tensor")),
        P("dp", "tensor"),
        P("tensor", "dp"),
        P("tensor", "dp"),
        P(("dp", "tensor")),
        P("dp", "tensor"),
        P("tensor", "dp"),
        P("tensor", "dp"),
        P(("dp", "tensor")),
    )
    return jax.shard_map(local, mesh=mesh, in_specs=in_specs, out_specs=out_specs, check_vma=False)
```
